256 devices in a mesh: dp: 16 (over x_lo, z), space: 16 (over x_hi, y, core).
Axes of the slice: x: 4 (x_hi: 2, x_lo: 2; x = x_hi * 2 + x_lo), y: 4, z: 8, core: 2. Of those that a mesh axis runs over, the one named last changes fastest.
Arguments:
- volume: bfloat16 [16, 4, 64, 8, 512], P('dp', None, 'space'), may hold values from -6 to 6
- cotangent: bfloat16 [16, 32, 16, 2, 128], P('dp', None, 'space'), may hold values from -1 to 1
- w_first: bfloat16 [16, 4, 3, 3, 3], replicated, may hold values from -0.625 to 0.625
- b_first: float32 [16], replicated, may hold values from -3 to 3
- w_second: bfloat16 [32, 16, 3, 3, 3], replicated, may hold values from -0.3125 to 0.3125
- b_second: float32 [32], replicated, may hold values from -3 to 3
Outputs:
- output: bfloat16 [16, 32, 16, 2, 128], P('dp', None, 'space')
- grad_w_first: float32 [16, 4, 3, 3, 3], replicated
- grad_b_first: float32 [16], replicated
- grad_w_second: float32 [32, 16, 3, 3, 3], replicated
- grad_b_second: float32 [32], replicated
The draws below stay inside these ranges and needn't reach their ends.
All inputs are finite; a program needn't handle non-finite values.
Results may differ from the reference program's by a relative error of at most 0.0047.
Values may be sent and summed in bfloat16 or wider, within the bound.
No kernel may reach another device: no remote copies, remote signals or barrier semaphores. Data moves between devices by JAX's collectives and lax.ppermute only.
A program may use at most 128 MiB of HBM per device.

```python
import math
import jax
import jax.numpy as jnp
from jax import lax

C0 = 4
C1 = 16
C2 = 32
Y = 8
Z = 512
X = 64
B = 16


def draw_cotangent(key, part):
    shape = (B, C2, X // 4, Y // 4, Z // 4)
    total = B * X * Y * Z
    base = 80.0 / math.sqrt(total)
    layer = jnp.arange(X // 4, dtype=jnp.float32) / max(X // 4 - 1, 1)
    rising = (3.0 ** layer)[None, None, :, None, None]
    sample = jnp.arange(B, dtype=jnp.float32) / max(B - 1, 1)
    sample_scale = (2.0 ** sample)[:, None, None, None, None]
    values = jax.random.normal(key, shape, jnp.float32)
    return jnp.clip(values * base * rising * sample_scale, -1.0, 1.0).astype(jnp.bfloat16)


def levels(key, dims, shards, smallest, top_value):
    loudness, own = 1.0, jax.random.fold_in(key, 6)
    for position, shards_of in shards:
        heights = jnp.exp(jax.random.uniform(jax.random.fold_in(own, position), (shards_of,), jnp.float32, smallest / len(shards), top_value / len(shards)))
        loudness = loudness * jnp.repeat(heights, dims[position] // shards_of).reshape([-1 if axis == position else 1 for axis in range(len(dims))])
    return loudness


def scatter_about(own_key, shape, scale, reach, cuts=(), kind=jnp.bfloat16):
    entries = scale * jax.random.normal(own_key, shape, jnp.float32)
    if cuts:
        entries = entries * levels(own_key, shape, cuts, -0.22, 0.18)
    return jnp.clip(entries, -reach, reach).astype(kind)


def setup_inputs(seed: int = 0) -> dict:
    arg_keys = jax.random.split(jax.random.key(seed), 7)
    return {
        "volume": scatter_about(arg_keys[0], (B, C0, X, Y, Z), 1.0, 6.0, ((0, 16), (2, 16))),
        "cotangent": draw_cotangent(jax.random.fold_in(arg_keys[6], 71), 0),
        "w_first": scatter_about(arg_keys[2], (C1, C0, 3, 3, 3), (C0 * 27) ** -0.5, 0.625),
        "b_first": scatter_about(arg_keys[3], (C1,), 0.5, 3.0, (), jnp.float32),
        "w_second": scatter_about(arg_keys[4], (C2, C1, 3, 3, 3), (C1 * 27) ** -0.5, 0.3125),
        "b_second": scatter_about(arg_keys[5], (C2,), 0.5, 3.0, (), jnp.float32),
    }


def conv_valid(inp, kern):
    return lax.conv_general_dilated(inp[None], kern, (1, 1, 1), 'VALID', dimension_numbers=('NCDHW', 'OIDHW', 'NCDHW'), precision=lax.Precision.HIGHEST, preferred_element_type=jnp.float32)[0]

def pad_all(field):
    return jnp.pad(field, ((0, 0), (1, 1), (1, 1), (1, 1)))

def avg_pool(field):
    chan, depth, height, width = field.shape
    return field.reshape(chan, depth // 2, 2, height // 2, 2, width // 2, 2).mean(axis=(2, 4, 6))

def upsample(field):
    return jnp.repeat(jnp.repeat(jnp.repeat(field, 2, axis=1), 2, axis=2), 2, axis=3)

def silu_slope(value):
    sig = jax.nn.sigmoid(value)
    return sig * (1.0 + value * (1.0 - sig))

def weight_grad(padded, grads):
    depth, height, width = grads.shape[1:]
    taps = []
    for depth_at in range(3):
        for row_at in range(3):
            for col_at in range(3):
                piece = padded[:, depth_at:depth_at + depth, row_at:row_at + height, col_at:col_at + width]
                taps.append(jnp.einsum('oxyz,cxyz->oc', grads, piece, precision=lax.Precision.HIGHEST))
    stacked = jnp.stack(taps, axis=-1)
    return stacked.reshape(grads.shape[0], padded.shape[0], 3, 3, 3)

def reference(volume, cotangent, w_first, b_first, w_second, b_second):
    kern_first = w_first.astype(jnp.float32)
    kern_second = w_second.astype(jnp.float32)
    flipped = jnp.transpose(jnp.flip(kern_second, (2, 3, 4)), (1, 0, 2, 3, 4))

    def one_sample(pair):
        sample, cot = pair
        padded_input = pad_all(sample.astype(jnp.float32))
        pre_first = conv_valid(padded_input, kern_first) + b_first[:, None, None, None]
        pooled = avg_pool(jax.nn.silu(pre_first)).astype(jnp.bfloat16)
        pooled = lax.optimization_barrier(pooled)
        padded_pool = pad_all(pooled.astype(jnp.float32))
        pre_second = conv_valid(padded_pool, kern_second) + b_second[:, None, None, None]
        output = avg_pool(jax.nn.silu(pre_second)).astype(jnp.bfloat16)
        grad_second = (upsample(cot.astype(jnp.float32)) * 0.125 * silu_slope(pre_second)).astype(jnp.bfloat16)
        grad_second = lax.optimization_barrier(grad_second).astype(jnp.float32)
        grad_w2 = weight_grad(padded_pool, grad_second)
        grad_b2 = lax.optimization_barrier(jnp.sum(grad_second, axis=(1, 2, 3)))
        back = conv_valid(pad_all(grad_second), flipped)
        grad_first = (upsample(back) * 0.125 * silu_slope(pre_first)).astype(jnp.bfloat16)
        grad_first = lax.optimization_barrier(grad_first).astype(jnp.float32)
        grad_w1 = weight_grad(padded_input, grad_first)
        grad_b1 = lax.optimization_barrier(jnp.sum(grad_first, axis=(1, 2, 3)))
        return (output, grad_w1, grad_b1, grad_w2, grad_b2)
    results = lax.map(one_sample, (volume, cotangent))
    return (results[0], lax.optimization_barrier(jnp.sum(results[1], axis=0)), lax.optimization_barrier(jnp.sum(results[2], axis=0)), lax.optimization_barrier(jnp.sum(results[3], axis=0)), lax.optimization_barrier(jnp.sum(results[4], axis=0)))
```

```python
import jax
import jax.numpy as jnp
from jax import lax
from jax.sharding import PartitionSpec as P


def with_halo(cells, sides, width):
    for axis, dim in sides:
        count = lax.axis_size(axis)
        ends = count - 1
        head = lax.slice_in_dim(cells, 0, width, axis=dim)
        tail = lax.slice_in_dim(cells, cells.shape[dim] - width, cells.shape[dim], axis=dim)
        cells = jnp.concatenate(
            [
                lax.ppermute(tail, axis, [(i, (i + 1) % count) for i in range(ends)]),
                cells,
                lax.ppermute(head, axis, [((i + 1) % count, i) for i in range(ends)]),
            ],
            axis=dim,
        )
    return cells


def conv_valid(inp, kern):
    return lax.conv_general_dilated(
        inp[None],
        kern,
        (1, 1, 1),
        "VALID",
        dimension_numbers=("NCDHW", "OIDHW", "NCDHW"),
        preferred_element_type=jnp.float32,
    )[0]


def pad_sides(field):
    return jnp.pad(field, ((0, 0), (0, 0), (1, 1), (1, 1)))


def avg_pool(field):
    chan, depth, height, width = field.shape
    return field.reshape(chan, depth // 2, 2, height // 2, 2, width // 2, 2).mean(axis=(2, 4, 6))


def upsample(field):
    return jnp.repeat(jnp.repeat(jnp.repeat(field, 2, axis=1), 2, axis=2), 2, axis=3)


def silu_slope(value):
    sig = jax.nn.sigmoid(value)
    return sig * (1.0 + value * (1.0 - sig))


def weight_grad(padded, grads):
    depth, height, width = grads.shape[1:]
    taps = []
    for depth_at in range(3):
        for row_at in range(3):
            for col_at in range(3):
                piece = padded[
                    :,
                    depth_at : depth_at + depth,
                    row_at : row_at + height,
                    col_at : col_at + width,
                ]
                taps.append(
                    jnp.einsum("oxyz,cxyz->oc", grads, piece, preferred_element_type=jnp.float32)
                )
    stacked = jnp.stack(taps, axis=-1)
    return stacked.reshape(grads.shape[0], padded.shape[0], 3, 3, 3)


def butterfly_sum(parts, axes):
    flat = jnp.concatenate([part.reshape(-1) for part in parts])
    for axis in axes:
        count = lax.axis_size(axis)
        step = 1
        while step < count:
            flat = flat + lax.ppermute(flat, axis, [(i, i ^ step) for i in range(count)])
            step *= 2
    sums, start = [], 0
    for part in parts:
        sums.append(flat[start : start + part.size].reshape(part.shape))
        start += part.size
    return tuple(sums)


def shards(volume, cotangent, w_first, b_first, w_second, b_second):
    sample = volume[0]
    cot = cotangent[0]
    padded_input = pad_sides(with_halo(sample, (("space", 1),), 1))
    pre_first = conv_valid(padded_input, w_first) + b_first[:, None, None, None]
    pooled = avg_pool(jax.nn.silu(pre_first)).astype(jnp.bfloat16)
    padded_pool = pad_sides(with_halo(pooled, (("space", 1),), 1))
    pre_second = conv_valid(padded_pool, w_second) + b_second[:, None, None, None]
    grad_second = (upsample(cot.astype(jnp.float32)) * 0.125 * silu_slope(pre_second)).astype(
        jnp.bfloat16
    )
    padded_grad = pad_sides(with_halo(grad_second, (("space", 1),), 1))
    output = avg_pool(jax.nn.silu(pre_second)).astype(jnp.bfloat16)
    grad_w2 = weight_grad(padded_pool, grad_second)
    grad_b2 = jnp.sum(grad_second.astype(jnp.float32), axis=(1, 2, 3))
    flipped = jnp.transpose(jnp.flip(w_second, (2, 3, 4)), (1, 0, 2, 3, 4))
    back = conv_valid(padded_grad, flipped)
    grad_first = (upsample(back) * 0.125 * silu_slope(pre_first)).astype(jnp.bfloat16)
    grad_w1 = weight_grad(padded_input, grad_first)
    grad_b1 = jnp.sum(grad_first.astype(jnp.float32), axis=(1, 2, 3))
    totals = butterfly_sum((grad_w1, grad_b1, grad_w2, grad_b2), ("space", "dp"))
    return (output[None], totals[0], totals[1], totals[2], totals[3])


def solution(mesh):
    placed = (
        P("dp", None, "space", None, None),
        P("dp", None, "space", None, None),
        P(),
        P(),
        P(),
        P(),
    )
    return jax.shard_map(
        shards,
        mesh=mesh,
        in_specs=placed,
        out_specs=(P("dp", None, "space", None, None), P(), P(), P(), P()),
        check_vma=False,
    )
```

```python
import jax
import jax.numpy as jnp
from jax import lax
from jax.sharding import PartitionSpec as P


def with_halo(cells, axis, dim):
    count = lax.axis_size(axis)
    ends = count - 1
    head = lax.slice_in_dim(cells, 0, 1, axis=dim)
    tail = lax.slice_in_dim(cells, cells.shape[dim] - 1, cells.shape[dim], axis=dim)
    return jnp.concatenate(
        [
            lax.ppermute(tail, axis, [(i, (i + 1) % count) for i in range(ends)]),
            cells,
            lax.ppermute(head, axis, [((i + 1) % count, i) for i in range(ends)]),
        ],
        axis=dim,
    )


def lane_shift(field, dm):
    if dm == 0:
        return field
    zeros = jnp.zeros(field.shape[:-1] + (1,), field.dtype)
    if dm < 0:
        return jnp.concatenate([zeros, field[..., :-1]], axis=-1)
    return jnp.concatenate([field[..., 1:], zeros], axis=-1)


def phase_patches(field):
    phases, _, depth, height, width = field.shape
    depth -= 2
    field = jnp.pad(field, ((0, 0), (0, 0), (0, 0), (1, 1), (0, 0)))
    sources = {}
    for r in range(phases):
        for e in range(3):
            key = ((r + e - 1) % phases, (r + e - 1) // phases)
            if key not in sources:
                sources[key] = lane_shift(field[key[0]], key[1])
    keys = sorted(sources)
    rows = {}
    for key in keys:
        for b in range(3):
            rows[key + (b,)] = sources[key][:, :, b : b + height, :]
    names = sorted(rows)
    rows = dict(zip(names, lax.optimization_barrier(tuple(rows[n] for n in names))))
    out = []
    for r in range(phases):
        taps = []
        for a in range(3):
            for b in range(3):
                for e in range(3):
                    key = ((r + e - 1) % phases, (r + e - 1) // phases, b)
                    taps.append(rows[key][:, a : a + depth])
        out.append(jnp.stack(taps, axis=0))
    return jnp.stack(out, axis=0)


def conv_taps(kern, patches):
    return jnp.einsum("otc,rtcxym->orxym", kern, patches, preferred_element_type=jnp.float32)


def grad_taps(grads, patches):
    return jnp.einsum("orxym,rtcxym->otc", grads, patches, preferred_element_type=jnp.float32)


def pool(field):
    chan, phases, depth, height, width = field.shape
    blocks = field.reshape(chan, phases // 2, 2, depth // 2, 2, height // 2, 2, width)
    return blocks.sum(axis=(2, 4, 6)) * 0.125


def upsample(field, phases):
    return jnp.repeat(jnp.repeat(jnp.repeat(field, 2, axis=1), 2, axis=2), 2, axis=3)


def silu_slope(value):
    sig = jax.nn.sigmoid(value)
    return sig * (1.0 + value * (1.0 - sig))


def butterfly_sum(parts, axes):
    flat = jnp.concatenate([part.reshape(-1) for part in parts])
    for axis in axes:
        count = lax.axis_size(axis)
        step = 1
        while step < count:
            flat = flat + lax.ppermute(flat, axis, [(i, i ^ step) for i in range(count)])
            step *= 2
    sums, start = [], 0
    for part in parts:
        sums.append(flat[start : start + part.size].reshape(part.shape))
        start += part.size
    return tuple(sums)


def tap_major(kern):
    return jnp.transpose(kern, (0, 2, 3, 4, 1)).reshape(kern.shape[0], 27, kern.shape[1])


def tap_minor(grad, chan):
    return jnp.transpose(grad.reshape(grad.shape[0], 3, 3, 3, chan), (0, 4, 1, 2, 3))


def shards(volume, cotangent, w_first, b_first, w_second, b_second):
    sample = volume[0]
    cot = cotangent[0]
    chan0, _, height, width = sample.shape
    halo = with_halo(sample, "space", 1)
    split = jnp.moveaxis(halo.reshape(chan0, halo.shape[1], height, width // 4, 4), 4, 0)
    patches_first = phase_patches(split)
    pre_first = conv_taps(tap_major(w_first), patches_first) + b_first[:, None, None, None, None]
    pooled = pool(jax.nn.silu(pre_first)).astype(jnp.bfloat16)
    pooled_halo = jnp.moveaxis(with_halo(pooled, "space", 2), 1, 0)
    patches_second = phase_patches(pooled_halo)
    pre_second = conv_taps(tap_major(w_second), patches_second) + b_second[:, None, None, None, None]
    output = pool(jax.nn.silu(pre_second))[:, 0].astype(jnp.bfloat16)
    grad_second = (
        upsample(cot.astype(jnp.float32)[:, None], 2) * 0.125 * silu_slope(pre_second)
    ).astype(jnp.bfloat16)
    grad_w2 = grad_taps(grad_second, patches_second)
    grad_b2 = jnp.sum(grad_second.astype(jnp.float32), axis=(1, 2, 3, 4))
    grad_halo = jnp.moveaxis(with_halo(grad_second, "space", 2), 1, 0)
    flipped = tap_major(jnp.transpose(jnp.flip(w_second, (2, 3, 4)), (1, 0, 2, 3, 4)))
    back = conv_taps(flipped, phase_patches(grad_halo))
    grad_first = (upsample(back, 4) * 0.125 * silu_slope(pre_first)).astype(jnp.bfloat16)
    grad_w1 = grad_taps(grad_first, patches_first)
    grad_b1 = jnp.sum(grad_first.astype(jnp.float32), axis=(1, 2, 3, 4))
    totals = butterfly_sum(
        (tap_minor(grad_w1, chan0), grad_b1, tap_minor(grad_w2, w_second.shape[1]), grad_b2),
        ("space", "dp"),
    )
    return (output[None], totals[0], totals[1], totals[2], totals[3])


def solution(mesh):
    placed = (
        P("dp", None, "space", None, None),
        P("dp", None, "space", None, None),
        P(),
        P(),
        P(),
        P(),
    )
    return jax.shard_map(
        shards,
        mesh=mesh,
        in_specs=placed,
        out_specs=(P("dp", None, "space", None, None), P(), P(), P(), P()),
        check_vma=False,
    )
```

```python
import jax
import jax.numpy as jnp
from jax import lax
from jax.sharding import PartitionSpec as P


def with_halo(cells, axis, dim):
    count = lax.axis_size(axis)
    ends = count - 1
    head = lax.slice_in_dim(cells, 0, 1, axis=dim)
    tail = lax.slice_in_dim(cells, cells.shape[dim] - 1, cells.shape[dim], axis=dim)
    return jnp.concatenate(
        [
            lax.ppermute(tail, axis, [(i, (i + 1) % count) for i in range(ends)]),
            cells,
            lax.ppermute(head, axis, [((i + 1) % count, i) for i in range(ends)]),
        ],
        axis=dim,
    )


def lane_shift(field, dm):
    if dm == 0:
        return field
    zeros = jnp.zeros(field.shape[:-1] + (1,), field.dtype)
    if dm < 0:
        return jnp.concatenate([zeros, field[..., :-1]], axis=-1)
    return jnp.concatenate([field[..., 1:], zeros], axis=-1)


def phase_patches(field):
    phases, depth, height, _, width = field.shape
    depth -= 2
    field = jnp.pad(field, ((0, 0), (0, 0), (1, 1), (0, 0), (0, 0)))
    sources = {}
    out = []
    for r in range(phases):
        taps = []
        for a in range(3):
            for b in range(3):
                for e in range(3):
                    key = ((r + e - 1) % phases, (r + e - 1) // phases)
                    if key not in sources:
                        sources[key] = lane_shift(field[key[0]], key[1])
                    taps.append(sources[key][a : a + depth, b : b + height])
        out.append(jnp.concatenate(taps, axis=2))
    return jnp.stack(out, axis=0)


def conv_taps(kern, patches):
    return jnp.einsum("ok,rxykm->orxym", kern.reshape(kern.shape[0], -1), patches, preferred_element_type=jnp.float32)


def grad_taps(grads, patches):
    return jnp.einsum("orxym,rxykm->ok", grads, patches, preferred_element_type=jnp.float32)


def pool(field):
    chan, phases, depth, height, width = field.shape
    blocks = field.reshape(chan, phases // 2, 2, depth // 2, 2, height // 2, 2, width)
    return blocks.sum(axis=(2, 4, 6)) * 0.125


def upsample(field, phases):
    return jnp.repeat(jnp.repeat(jnp.repeat(field, 2, axis=1), 2, axis=2), 2, axis=3)


def silu_slope(value):
    sig = jax.nn.sigmoid(value)
    return sig * (1.0 + value * (1.0 - sig))


def butterfly_sum(parts, axes):
    flat = jnp.concatenate([part.reshape(-1) for part in parts])
    for axis in axes:
        count = lax.axis_size(axis)
        step = 1
        while step < count:
            flat = flat + lax.ppermute(flat, axis, [(i, i ^ step) for i in range(count)])
            step *= 2
    sums, start = [], 0
    for part in parts:
        sums.append(flat[start : start + part.size].reshape(part.shape))
        start += part.size
    return tuple(sums)


def tap_major(kern):
    return jnp.transpose(kern, (0, 2, 3, 4, 1)).reshape(kern.shape[0], 27, kern.shape[1])


def tap_minor(grad, chan):
    return jnp.transpose(grad.reshape(grad.shape[0], 3, 3, 3, chan), (0, 4, 1, 2, 3))


def shards(volume, cotangent, w_first, b_first, w_second, b_second):
    sample = volume[0]
    cot = cotangent[0]
    chan0, _, height, width = sample.shape
    halo = with_halo(sample, "space", 1)
    split = jnp.transpose(halo.reshape(chan0, halo.shape[1], height, width // 4, 4), (4, 1, 2, 0, 3))
    patches_first = phase_patches(split)
    pre_first = conv_taps(tap_major(w_first), patches_first) + b_first[:, None, None, None, None]
    pooled = pool(jax.nn.silu(pre_first)).astype(jnp.bfloat16)
    pooled_halo = jnp.transpose(with_halo(pooled, "space", 2), (1, 2, 3, 0, 4))
    patches_second = phase_patches(pooled_halo)
    pre_second = conv_taps(tap_major(w_second), patches_second) + b_second[:, None, None, None, None]
    output = pool(jax.nn.silu(pre_second))[:, 0].astype(jnp.bfloat16)
    grad_second = (
        upsample(cot.astype(jnp.float32)[:, None], 2) * 0.125 * silu_slope(pre_second)
    ).astype(jnp.bfloat16)
    grad_w2 = grad_taps(grad_second, patches_second)
    grad_b2 = jnp.sum(grad_second.astype(jnp.float32), axis=(1, 2, 3, 4))
    grad_halo = jnp.transpose(with_halo(grad_second, "space", 2), (1, 2, 3, 0, 4))
    flipped = tap_major(jnp.transpose(jnp.flip(w_second, (2, 3, 4)), (1, 0, 2, 3, 4)))
    back = conv_taps(flipped, phase_patches(grad_halo))
    grad_first = (upsample(back, 4) * 0.125 * silu_slope(pre_first)).astype(jnp.bfloat16)
    grad_w1 = grad_taps(grad_first, patches_first)
    grad_b1 = jnp.sum(grad_first.astype(jnp.float32), axis=(1, 2, 3, 4))
    totals = butterfly_sum(
        (tap_minor(grad_w1, chan0), grad_b1, tap_minor(grad_w2, w_second.shape[1]), grad_b2),
        ("space", "dp"),
    )
    return (output[None], totals[0], totals[1], totals[2], totals[3])


def solution(mesh):
    placed = (
        P("dp", None, "space", None, None),
        P("dp", None, "space", None, None),
        P(),
        P(),
        P(),
        P(),
    )
    return jax.shard_map(
        shards,
        mesh=mesh,
        in_specs=placed,
        out_specs=(P("dp", None, "space", None, None), P(), P(), P(), P()),
        check_vma=False,
    )
```

```python
import jax
import jax.numpy as jnp
from jax import lax
from jax.sharding import PartitionSpec as P


def with_halo(cells, axis, dim):
    count = lax.axis_size(axis)
    ends = count - 1
    head = lax.slice_in_dim(cells, 0, 1, axis=dim)
    tail = lax.slice_in_dim(cells, cells.shape[dim] - 1, cells.shape[dim], axis=dim)
    return jnp.concatenate(
        [
            lax.ppermute(tail, axis, [(i, (i + 1) % count) for i in range(ends)]),
            cells,
            lax.ppermute(head, axis, [((i + 1) % count, i) for i in range(ends)]),
        ],
        axis=dim,
    )


def lane_shift(field, dm):
    if dm == 0:
        return field
    zeros = jnp.zeros(field.shape[:-1] + (1,), field.dtype)
    if dm < 0:
        return jnp.concatenate([zeros, field[..., :-1]], axis=-1)
    return jnp.concatenate([field[..., 1:], zeros], axis=-1)


def phase_patches(field):
    phases, depth, height, _, width = field.shape
    depth -= 2
    field = jnp.pad(field, ((0, 0), (0, 0), (1, 1), (0, 0), (0, 0)))
    keys = sorted({((r + e - 1) % phases, (r + e - 1) // phases) for r in range(phases) for e in range(3)})
    moved = [key for key in keys if key[1] != 0]
    shifted = lax.optimization_barrier(tuple(lane_shift(field[key[0]], key[1]) for key in moved))
    sources = {key: field[key[0]] for key in keys if key[1] == 0}
    sources.update(zip(moved, shifted))
    out = []
    for r in range(phases):
        taps = []
        for a in range(3):
            for b in range(3):
                for e in range(3):
                    key = ((r + e - 1) % phases, (r + e - 1) // phases)
                    taps.append(sources[key][a : a + depth, b : b + height])
        out.append(jnp.concatenate(taps, axis=2))
    return jnp.stack(out, axis=0)


def conv_taps(kern, patches):
    return jnp.einsum("ok,rxykm->orxym", kern.reshape(kern.shape[0], -1), patches, preferred_element_type=jnp.float32)


def grad_taps(grads, patches):
    return jnp.einsum("orxym,rxykm->ok", grads, patches, preferred_element_type=jnp.float32)


def pool(field):
    chan, phases, depth, height, width = field.shape
    blocks = field.reshape(chan, phases // 2, 2, depth // 2, 2, height // 2, 2, width)
    return blocks.sum(axis=(2, 4, 6)) * 0.125


def upsample(field, phases):
    return jnp.repeat(jnp.repeat(jnp.repeat(field, 2, axis=1), 2, axis=2), 2, axis=3)


def silu_slope(value):
    sig = jax.nn.sigmoid(value)
    return sig * (1.0 + value * (1.0 - sig))


def butterfly_sum(rows, axes):
    for axis in axes:
        count = lax.axis_size(axis)
        step = 1
        while step < count:
            rows = rows + lax.ppermute(rows, axis, [(i, i ^ step) for i in range(count)])
            step *= 2
    return rows


def tap_major(kern):
    return jnp.transpose(kern, (0, 2, 3, 4, 1)).reshape(kern.shape[0], 27, kern.shape[1])


def tap_minor(grad, chan):
    return jnp.transpose(grad.reshape(grad.shape[0], 3, 3, 3, chan), (0, 4, 1, 2, 3))


def shards(volume, cotangent, w_first, b_first, w_second, b_second):
    sample = volume[0]
    cot = cotangent[0]
    chan0, _, height, width = sample.shape
    halo = with_halo(sample, "space", 1)
    split = jnp.transpose(halo.reshape(chan0, halo.shape[1], height, width // 4, 4), (4, 1, 2, 0, 3))
    patches_first = phase_patches(split)
    pre_first = conv_taps(tap_major(w_first), patches_first) + b_first[:, None, None, None, None]
    pooled = pool(jax.nn.silu(pre_first)).astype(jnp.bfloat16)
    pooled_halo = jnp.transpose(with_halo(pooled, "space", 2), (1, 2, 3, 0, 4))
    patches_second = phase_patches(pooled_halo)
    pre_second = conv_taps(tap_major(w_second), patches_second) + b_second[:, None, None, None, None]
    output = pool(jax.nn.silu(pre_second))[:, 0].astype(jnp.bfloat16)
    grad_second = (
        upsample(cot.astype(jnp.float32)[:, None], 2) * 0.125 * silu_slope(pre_second)
    ).astype(jnp.bfloat16)
    grad_w2 = grad_taps(grad_second, patches_second)
    grad_b2 = jnp.sum(grad_second.astype(jnp.float32), axis=(1, 2, 3, 4))
    grad_halo = jnp.transpose(with_halo(grad_second, "space", 2), (1, 2, 3, 0, 4))
    flipped = tap_major(jnp.transpose(jnp.flip(w_second, (2, 3, 4)), (1, 0, 2, 3, 4)))
    back = conv_taps(flipped, phase_patches(grad_halo))
    grad_first = (upsample(back, 4) * 0.125 * silu_slope(pre_first)).astype(jnp.bfloat16)
    grad_w1 = grad_taps(grad_first, patches_first)
    grad_b1 = jnp.sum(grad_first.astype(jnp.float32), axis=(1, 2, 3, 4))
    chan1 = w_second.shape[1]
    lanes = grad_w2.shape[1]
    biases = jnp.concatenate([grad_b1, grad_b2])
    rows = jnp.concatenate(
        [
            grad_w2,
            jnp.pad(grad_w1, ((0, 0), (0, lanes - grad_w1.shape[1]))),
            jnp.pad(biases, (0, lanes - biases.shape[0]))[None],
        ]
    )
    totals = butterfly_sum(rows, ("space", "dp"))
    out_w2 = tap_minor(totals[: grad_w2.shape[0]], chan1)
    out_w1 = tap_minor(totals[grad_w2.shape[0] : -1, : grad_w1.shape[1]], chan0)
    out_b1 = totals[-1, : grad_b1.shape[0]]
    out_b2 = totals[-1, grad_b1.shape[0] : biases.shape[0]]
    return (output[None], out_w1, out_b1, out_w2, out_b2)


def solution(mesh):
    placed = (
        P("dp", None, "space", None, None),
        P("dp", None, "space", None, None),
        P(),
        P(),
        P(),
        P(),
    )
    return jax.shard_map(
        shards,
        mesh=mesh,
        in_specs=placed,
        out_specs=(P("dp", None, "space", None, None), P(), P(), P(), P()),
        check_vma=False,
    )
```

```python
import jax
import numpy as np
import jax.numpy as jnp
from jax import lax
from jax.sharding import PartitionSpec as P


def with_halo(cells, axis, dim):
    count = lax.axis_size(axis)
    ends = count - 1
    head = lax.slice_in_dim(cells, 0, 1, axis=dim)
    tail = lax.slice_in_dim(cells, cells.shape[dim] - 1, cells.shape[dim], axis=dim)
    return jnp.concatenate(
        [
            lax.ppermute(tail, axis, [(i, (i + 1) % count) for i in range(ends)]),
            cells,
            lax.ppermute(head, axis, [((i + 1) % count, i) for i in range(ends)]),
        ],
        axis=dim,
    )


def lane_shift(field, dm):
    if dm == 0:
        return field
    zeros = jnp.zeros(field.shape[:-1] + (1,), field.dtype)
    if dm < 0:
        return jnp.concatenate([zeros, field[..., :-1]], axis=-1)
    return jnp.concatenate([field[..., 1:], zeros], axis=-1)


def phase_patches(field):
    phases, depth, height, _, width = field.shape
    depth -= 2
    field = jnp.pad(field, ((0, 0), (0, 0), (1, 1), (0, 0), (0, 0)))
    sources = {}
    out = []
    for r in range(phases):
        taps = []
        for a in range(3):
            for b in range(3):
                for e in range(3):
                    key = ((r + e - 1) % phases, (r + e - 1) // phases)
                    if key not in sources:
                        sources[key] = lane_shift(field[key[0]], key[1])
                    taps.append(sources[key][a : a + depth, b : b + height])
        out.append(jnp.concatenate(taps, axis=2))
    return jnp.stack(out, axis=0)


def conv_taps(kern, patches):
    return jnp.einsum("ok,rxykm->orxym", kern.reshape(kern.shape[0], -1), patches, preferred_element_type=jnp.float32)


def grad_taps(grads, patches):
    return jnp.einsum("orxym,rxykm->ok", grads, patches, preferred_element_type=jnp.float32)


def pool(field):
    chan, phases, depth, height, width = field.shape
    blocks = field.reshape(chan, phases // 2, 2, depth // 2, 2, height // 2, 2, width)
    return blocks.sum(axis=(2, 4, 6)) * 0.125


def upsample(field, phases):
    return jnp.repeat(jnp.repeat(jnp.repeat(field, 2, axis=1), 2, axis=2), 2, axis=3)


def silu_slope(value):
    sig = jax.nn.sigmoid(value)
    return sig * (1.0 + value * (1.0 - sig))


def butterfly_sum(rows, axes):
    for axis in axes:
        count = lax.axis_size(axis)
        step = 1
        while step < count:
            rows = rows + lax.ppermute(rows, axis, [(i, i ^ step) for i in range(count)])
            step *= 2
    return rows


def tap_major(kern):
    return jnp.transpose(kern, (0, 2, 3, 4, 1)).reshape(kern.shape[0], 27, kern.shape[1])


def tap_minor(grad, chan):
    return jnp.transpose(grad.reshape(grad.shape[0], 3, 3, 3, chan), (0, 4, 1, 2, 3))


def phase_select(phases):
    sel = np.zeros((phases, 3, phases, 3), np.float32)
    for r in range(phases):
        for e in range(3):
            sel[r, (r + e - 1) // phases + 1, (r + e - 1) % phases, e] = 1.0
    return sel


def merged_patches(field):
    depth, height = field.shape[0] - 2, field.shape[1]
    field = jnp.pad(field, ((0, 0), (1, 1), (0, 0), (0, 0)))
    shifted = [lane_shift(field, dm) for dm in (-1, 0, 1)]
    taps = []
    for a in range(3):
        for b in range(3):
            for dm in range(3):
                taps.append(shifted[dm][a : a + depth, b : b + height])
    return jnp.concatenate(taps, axis=2)


def merged_kernel(kern, phases):
    sel = phase_select(phases)
    taps = jnp.transpose(kern.astype(jnp.float32), (0, 2, 3, 1, 4))
    full = taps[:, None, :, :, None, None, :, :] * sel[None, :, None, None, :, :, None, :]
    return full.sum(axis=-1).reshape(kern.shape[0], phases, -1).astype(kern.dtype)


def merged_grad(grads, chan, phases):
    sel = phase_select(phases)
    full = grads.reshape(grads.shape[0], phases, 3, 3, 3, phases, chan)
    summed = (full[..., None] * sel[None, :, None, None, :, :, None, :]).sum(axis=(1, 4, 5))
    return jnp.transpose(summed, (0, 1, 2, 4, 3)).reshape(grads.shape[0], -1)


def shards(volume, cotangent, w_first, b_first, w_second, b_second):
    sample = volume[0]
    cot = cotangent[0]
    chan0, _, height, width = sample.shape
    halo = with_halo(sample, "space", 1)
    merged = jnp.transpose(halo.reshape(chan0, halo.shape[1], height, width // 4, 4), (1, 2, 4, 0, 3))
    patches_first = merged_patches(merged.reshape(halo.shape[1], height, 4 * chan0, width // 4))
    pre_first = (
        jnp.einsum(
            "ork,xykm->orxym", merged_kernel(w_first, 4), patches_first, preferred_element_type=jnp.float32
        )
        + b_first[:, None, None, None, None]
    )
    pooled = pool(jax.nn.silu(pre_first)).astype(jnp.bfloat16)
    pooled_halo = jnp.transpose(with_halo(pooled, "space", 2), (1, 2, 3, 0, 4))
    patches_second = phase_patches(pooled_halo)
    pre_second = conv_taps(tap_major(w_second), patches_second) + b_second[:, None, None, None, None]
    output = pool(jax.nn.silu(pre_second))[:, 0].astype(jnp.bfloat16)
    grad_second = (
        upsample(cot.astype(jnp.float32)[:, None], 2) * 0.125 * silu_slope(pre_second)
    ).astype(jnp.bfloat16)
    grad_w2 = grad_taps(grad_second, patches_second)
    grad_b2 = jnp.sum(grad_second.astype(jnp.float32), axis=(1, 2, 3, 4))
    grad_halo = jnp.transpose(with_halo(grad_second, "space", 2), (1, 2, 3, 0, 4))
    flipped = tap_major(jnp.transpose(jnp.flip(w_second, (2, 3, 4)), (1, 0, 2, 3, 4)))
    back = conv_taps(flipped, phase_patches(grad_halo))
    grad_first = (upsample(back, 4) * 0.125 * silu_slope(pre_first)).astype(jnp.bfloat16)
    grad_w1 = merged_grad(
        jnp.einsum("orxym,xykm->ork", grad_first, patches_first, preferred_element_type=jnp.float32),
        chan0,
        4,
    )
    grad_b1 = jnp.sum(grad_first.astype(jnp.float32), axis=(1, 2, 3, 4))
    chan1 = w_second.shape[1]
    lanes = grad_w2.shape[1]
    biases = jnp.concatenate([grad_b1, grad_b2])
    rows = jnp.concatenate(
        [
            grad_w2,
            jnp.pad(grad_w1, ((0, 0), (0, lanes - grad_w1.shape[1]))),
            jnp.pad(biases, (0, lanes - biases.shape[0]))[None],
        ]
    )
    totals = butterfly_sum(rows, ("space", "dp"))
    out_w2 = tap_minor(totals[: grad_w2.shape[0]], chan1)
    out_w1 = tap_minor(totals[grad_w2.shape[0] : -1, : grad_w1.shape[1]], chan0)
    out_b1 = totals[-1, : grad_b1.shape[0]]
    out_b2 = totals[-1, grad_b1.shape[0] : biases.shape[0]]
    return (output[None], out_w1, out_b1, out_w2, out_b2)


def solution(mesh):
    placed = (
        P("dp", None, "space", None, None),
        P("dp", None, "space", None, None),
        P(),
        P(),
        P(),
        P(),
    )
    return jax.shard_map(
        shards,
        mesh=mesh,
        in_specs=placed,
        out_specs=(P("dp", None, "space", None, None), P(), P(), P(), P()),
        check_vma=False,
    )
```

```python
import jax
import numpy as np
import jax.numpy as jnp
from jax import lax
from jax.sharding import PartitionSpec as P


def with_halo(cells, axis, dim):
    count = lax.axis_size(axis)
    ends = count - 1
    head = lax.slice_in_dim(cells, 0, 1, axis=dim)
    tail = lax.slice_in_dim(cells, cells.shape[dim] - 1, cells.shape[dim], axis=dim)
    return jnp.concatenate(
        [
            lax.ppermute(tail, axis, [(i, (i + 1) % count) for i in range(ends)]),
            cells,
            lax.ppermute(head, axis, [((i + 1) % count, i) for i in range(ends)]),
        ],
        axis=dim,
    )


def lane_shift(field, dm):
    if dm == 0:
        return field
    zeros = jnp.zeros(field.shape[:-1] + (1,), field.dtype)
    if dm < 0:
        return jnp.concatenate([zeros, field[..., :-1]], axis=-1)
    return jnp.concatenate([field[..., 1:], zeros], axis=-1)


def phase_patches(field):
    phases, depth, height, _, width = field.shape
    depth -= 2
    field = jnp.pad(field, ((0, 0), (0, 0), (1, 1), (0, 0), (0, 0)))
    sources = {}
    out = []
    for r in range(phases):
        taps = []
        for a in range(3):
            for b in range(3):
                for e in range(3):
                    key = ((r + e - 1) % phases, (r + e - 1) // phases)
                    if key not in sources:
                        sources[key] = lane_shift(field[key[0]], key[1])
                    taps.append(sources[key][a : a + depth, b : b + height])
        out.append(jnp.concatenate(taps, axis=2))
    return jnp.stack(out, axis=0)


def conv_taps(kern, patches):
    return jnp.einsum("ok,rxykm->orxym", kern.reshape(kern.shape[0], -1), patches, preferred_element_type=jnp.float32)


def grad_taps(grads, patches):
    return jnp.einsum("orxym,rxykm->ok", grads, patches, preferred_element_type=jnp.float32)


def pool(field):
    chan, phases, depth, height, width = field.shape
    blocks = field.reshape(chan, phases // 2, 2, depth // 2, 2, height // 2, 2, width)
    return blocks.sum(axis=(2, 4, 6)) * 0.125


def upsample(field, phases):
    return jnp.repeat(jnp.repeat(jnp.repeat(field, 2, axis=1), 2, axis=2), 2, axis=3)


def silu_slope(value):
    sig = jax.nn.sigmoid(value)
    return sig * (1.0 + value * (1.0 - sig))


def butterfly_sum(rows, axes):
    for axis in axes:
        count = lax.axis_size(axis)
        step = 1
        while step < count:
            rows = rows + lax.ppermute(rows, axis, [(i, i ^ step) for i in range(count)])
            step *= 2
    return rows


def tap_major(kern):
    return jnp.transpose(kern, (0, 2, 3, 4, 1)).reshape(kern.shape[0], 27, kern.shape[1])


def tap_minor(grad, chan):
    return jnp.transpose(grad.reshape(grad.shape[0], 3, 3, 3, chan), (0, 4, 1, 2, 3))


def phase_select(phases):
    sel = np.zeros((phases, 3, phases, 3), np.float32)
    for r in range(phases):
        for e in range(3):
            sel[r, (r + e - 1) // phases + 1, (r + e - 1) % phases, e] = 1.0
    return sel


def merged_patches(field):
    depth, height = field.shape[0] - 2, field.shape[1]
    field = jnp.pad(field, ((0, 0), (1, 1), (0, 0), (0, 0)))
    shifted = [lane_shift(field, dm) for dm in (-1, 0, 1)]
    taps = []
    for a in range(3):
        for b in range(3):
            for dm in range(3):
                taps.append(shifted[dm][a : a + depth, b : b + height])
    return jnp.concatenate(taps, axis=2)


def merged_kernel(kern, phases):
    sel = phase_select(phases)
    taps = jnp.transpose(kern.astype(jnp.float32), (0, 2, 3, 1, 4))
    full = taps[:, None, :, :, None, None, :, :] * sel[None, :, None, None, :, :, None, :]
    return full.sum(axis=-1).reshape(kern.shape[0], phases, -1).astype(kern.dtype)


def merged_grad(grads, chan, phases):
    sel = phase_select(phases)
    full = grads.reshape(grads.shape[0], phases, 3, 3, 3, phases, chan)
    summed = (full[..., None] * sel[None, :, None, None, :, :, None, :]).sum(axis=(1, 4, 5))
    return jnp.transpose(summed, (0, 1, 2, 4, 3)).reshape(grads.shape[0], -1)


def shards(volume, cotangent, w_first, b_first, w_second, b_second):
    sample = volume[0]
    cot = cotangent[0]
    chan0, _, height, width = sample.shape
    halo = with_halo(sample, "space", 1)
    merged = jnp.transpose(halo.reshape(chan0, halo.shape[1], height, width // 4, 4), (1, 2, 4, 0, 3))
    patches_first = merged_patches(merged.reshape(halo.shape[1], height, 4 * chan0, width // 4))
    pre_first = (
        jnp.einsum(
            "ork,xykm->orxym", merged_kernel(w_first, 4), patches_first, preferred_element_type=jnp.float32
        )
        + b_first[:, None, None, None, None]
    )
    pooled = pool(jax.nn.silu(pre_first)).astype(jnp.bfloat16)
    pooled_halo = jnp.transpose(with_halo(pooled, "space", 2), (1, 2, 3, 0, 4))
    patches_second = phase_patches(pooled_halo)
    pre_second = conv_taps(tap_major(w_second), patches_second) + b_second[:, None, None, None, None]
    output = pool(jax.nn.silu(pre_second))[:, 0].astype(jnp.bfloat16)
    grad_second = (
        upsample(cot.astype(jnp.float32)[:, None], 2) * 0.125 * silu_slope(pre_second)
    ).astype(jnp.bfloat16)
    grad_w2 = grad_taps(grad_second, patches_second)
    grad_b2 = jnp.sum(grad_second.astype(jnp.float32), axis=(1, 2, 3, 4))
    grad_halo = jnp.transpose(with_halo(grad_second, "space", 2), (1, 2, 3, 0, 4))
    flipped = tap_major(jnp.transpose(jnp.flip(w_second, (2, 3, 4)), (1, 0, 2, 3, 4)))
    back = conv_taps(flipped, phase_patches(grad_halo))
    grad_first = (upsample(back, 4) * 0.125 * silu_slope(pre_first)).astype(jnp.bfloat16)
    grad_w1 = merged_grad(
        jnp.einsum("orxym,xykm->ork", grad_first, patches_first, preferred_element_type=jnp.float32),
        chan0,
        4,
    )
    grad_b1 = jnp.sum(grad_first.astype(jnp.float32), axis=(1, 2, 3, 4))
    chan1 = w_second.shape[1]
    rows_w2, lanes_w2 = grad_w2.shape
    side = grad_w1.reshape(rows_w2, -1)
    lanes_w1 = side.shape[1]
    packed = jnp.concatenate(
        [
            grad_w2,
            side,
            grad_b2[:, None],
            jnp.pad(grad_b1, (0, rows_w2 - grad_b1.shape[0]))[:, None],
        ],
        axis=1,
    )
    totals = butterfly_sum(packed, ("space", "dp"))
    out_w2 = tap_minor(totals[:, :lanes_w2], chan1)
    out_w1 = tap_minor(totals[:, lanes_w2 : lanes_w2 + lanes_w1].reshape(grad_w1.shape), chan0)
    out_b2 = totals[:, lanes_w2 + lanes_w1]
    out_b1 = totals[: grad_b1.shape[0], lanes_w2 + lanes_w1 + 1]
    return (output[None], out_w1, out_b1, out_w2, out_b2)


def solution(mesh):
    placed = (
        P("dp", None, "space", None, None),
        P("dp", None, "space", None, None),
        P(),
        P(),
        P(),
        P(),
    )
    return jax.shard_map(
        shards,
        mesh=mesh,
        in_specs=placed,
        out_specs=(P("dp", None, "space", None, None), P(), P(), P(), P()),
        check_vma=False,
    )
```

```python
import jax
import numpy as np
import jax.numpy as jnp
from jax import lax
from jax.sharding import PartitionSpec as P


def with_halo(cells, axis, dim, width=1):
    count = lax.axis_size(axis)
    ends = count - 1
    head = lax.slice_in_dim(cells, 0, width, axis=dim)
    tail = lax.slice_in_dim(cells, cells.shape[dim] - width, cells.shape[dim], axis=dim)
    return jnp.concatenate(
        [
            lax.ppermute(tail, axis, [(i, (i + 1) % count) for i in range(ends)]),
            cells,
            lax.ppermute(head, axis, [((i + 1) % count, i) for i in range(ends)]),
        ],
        axis=dim,
    )


def lane_shift(field, dm):
    if dm == 0:
        return field
    zeros = jnp.zeros(field.shape[:-1] + (1,), field.dtype)
    if dm < 0:
        return jnp.concatenate([zeros, field[..., :-1]], axis=-1)
    return jnp.concatenate([field[..., 1:], zeros], axis=-1)


def phase_patches(field):
    phases, depth, height, _, width = field.shape
    depth -= 2
    field = jnp.pad(field, ((0, 0), (0, 0), (1, 1), (0, 0), (0, 0)))
    sources = {}
    out = []
    for r in range(phases):
        taps = []
        for a in range(3):
            for b in range(3):
                for e in range(3):
                    key = ((r + e - 1) % phases, (r + e - 1) // phases)
                    if key not in sources:
                        sources[key] = lane_shift(field[key[0]], key[1])
                    taps.append(sources[key][a : a + depth, b : b + height])
        out.append(jnp.concatenate(taps, axis=2))
    return jnp.stack(out, axis=0)


def conv_taps(kern, patches):
    return jnp.einsum("ok,rxykm->orxym", kern.reshape(kern.shape[0], -1), patches, preferred_element_type=jnp.float32)


def grad_taps(grads, patches):
    return jnp.einsum("orxym,rxykm->ok", grads, patches, preferred_element_type=jnp.float32)


def pool(field):
    chan, phases, depth, height, width = field.shape
    blocks = field.reshape(chan, phases // 2, 2, depth // 2, 2, height // 2, 2, width)
    return blocks.sum(axis=(2, 4, 6)) * 0.125


def upsample(field, phases):
    return jnp.repeat(jnp.repeat(jnp.repeat(field, 2, axis=1), 2, axis=2), 2, axis=3)


def silu_slope(value):
    sig = jax.nn.sigmoid(value)
    return sig * (1.0 + value * (1.0 - sig))


def butterfly_sum(rows, axes):
    for axis in axes:
        count = lax.axis_size(axis)
        step = 1
        while step < count:
            rows = rows + lax.ppermute(rows, axis, [(i, i ^ step) for i in range(count)])
            step *= 2
    return rows


def tap_major(kern):
    return jnp.transpose(kern, (0, 2, 3, 4, 1)).reshape(kern.shape[0], 27, kern.shape[1])


def tap_minor(grad, chan):
    return jnp.transpose(grad.reshape(grad.shape[0], 3, 3, 3, chan), (0, 4, 1, 2, 3))


def phase_select(phases):
    sel = np.zeros((phases, 3, phases, 3), np.float32)
    for r in range(phases):
        for e in range(3):
            sel[r, (r + e - 1) // phases + 1, (r + e - 1) % phases, e] = 1.0
    return sel


def merged_patches(field):
    depth, height = field.shape[0] - 2, field.shape[1]
    field = jnp.pad(field, ((0, 0), (1, 1), (0, 0), (0, 0)))
    shifted = [lane_shift(field, dm) for dm in (-1, 0, 1)]
    taps = []
    for a in range(3):
        for b in range(3):
            for dm in range(3):
                taps.append(shifted[dm][a : a + depth, b : b + height])
    return jnp.concatenate(taps, axis=2)


def merged_kernel(kern, phases):
    sel = phase_select(phases)
    taps = jnp.transpose(kern.astype(jnp.float32), (0, 2, 3, 1, 4))
    full = taps[:, None, :, :, None, None, :, :] * sel[None, :, None, None, :, :, None, :]
    return full.sum(axis=-1).reshape(kern.shape[0], phases, -1).astype(kern.dtype)


def merged_grad(grads, chan, phases):
    sel = phase_select(phases)
    full = grads.reshape(grads.shape[0], phases, 3, 3, 3, phases, chan)
    summed = (full[..., None] * sel[None, :, None, None, :, :, None, :]).sum(axis=(1, 4, 5))
    return jnp.transpose(summed, (0, 1, 2, 4, 3)).reshape(grads.shape[0], -1)


def shards(volume, cotangent, w_first, b_first, w_second, b_second):
    sample = volume[0]
    cot = cotangent[0]
    chan0, _, height, width = sample.shape
    depth = sample.shape[1]
    halo = with_halo(sample, "space", 1, 3)
    merged = jnp.transpose(halo.reshape(chan0, halo.shape[1], height, width // 4, 4), (1, 2, 4, 0, 3))
    patches_wide = merged_patches(merged.reshape(halo.shape[1], height, 4 * chan0, width // 4))
    pre_wide = (
        jnp.einsum(
            "ork,xykm->orxym", merged_kernel(w_first, 4), patches_wide, preferred_element_type=jnp.float32
        )
        + b_first[:, None, None, None, None]
    )
    pooled_wide = pool(jax.nn.silu(pre_wide)).astype(jnp.bfloat16)
    place = lax.axis_index("space")
    rows = jnp.arange(pooled_wide.shape[2])
    inside = ((rows > 0) | (place > 0)) & ((rows < pooled_wide.shape[2] - 1) | (place < lax.axis_size("space") - 1))
    pooled_wide = jnp.where(inside[None, None, :, None, None], pooled_wide, jnp.zeros_like(pooled_wide))
    pooled_halo = jnp.transpose(pooled_wide, (1, 2, 3, 0, 4))
    pre_first = pre_wide[:, :, 2 : 2 + depth]
    patches_first = patches_wide[2 : 2 + depth]
    patches_second = phase_patches(pooled_halo)
    pre_second = conv_taps(tap_major(w_second), patches_second) + b_second[:, None, None, None, None]
    output = pool(jax.nn.silu(pre_second))[:, 0].astype(jnp.bfloat16)
    grad_second = (
        upsample(cot.astype(jnp.float32)[:, None], 2) * 0.125 * silu_slope(pre_second)
    ).astype(jnp.bfloat16)
    grad_w2 = grad_taps(grad_second, patches_second)
    grad_b2 = jnp.sum(grad_second.astype(jnp.float32), axis=(1, 2, 3, 4))
    grad_halo = jnp.transpose(with_halo(grad_second, "space", 2), (1, 2, 3, 0, 4))
    flipped = tap_major(jnp.transpose(jnp.flip(w_second, (2, 3, 4)), (1, 0, 2, 3, 4)))
    back = conv_taps(flipped, phase_patches(grad_halo))
    grad_first = (upsample(back, 4) * 0.125 * silu_slope(pre_first)).astype(jnp.bfloat16)
    grad_w1 = merged_grad(
        jnp.einsum("orxym,xykm->ork", grad_first, patches_first, preferred_element_type=jnp.float32),
        chan0,
        4,
    )
    grad_b1 = jnp.sum(grad_first.astype(jnp.float32), axis=(1, 2, 3, 4))
    chan1 = w_second.shape[1]
    rows_w2, lanes_w2 = grad_w2.shape
    side = grad_w1.reshape(rows_w2, -1)
    lanes_w1 = side.shape[1]
    packed = jnp.concatenate(
        [
            grad_w2,
            side,
            grad_b2[:, None],
            jnp.pad(grad_b1, (0, rows_w2 - grad_b1.shape[0]))[:, None],
        ],
        axis=1,
    )
    totals = butterfly_sum(packed, ("space", "dp"))
    out_w2 = tap_minor(totals[:, :lanes_w2], chan1)
    out_w1 = tap_minor(totals[:, lanes_w2 : lanes_w2 + lanes_w1].reshape(grad_w1.shape), chan0)
    out_b2 = totals[:, lanes_w2 + lanes_w1]
    out_b1 = totals[: grad_b1.shape[0], lanes_w2 + lanes_w1 + 1]
    return (output[None], out_w1, out_b1, out_w2, out_b2)


def solution(mesh):
    placed = (
        P("dp", None, "space", None, None),
        P("dp", None, "space", None, None),
        P(),
        P(),
        P(),
        P(),
    )
    return jax.shard_map(
        shards,
        mesh=mesh,
        in_specs=placed,
        out_specs=(P("dp", None, "space", None, None), P(), P(), P(), P()),
        check_vma=False,
    )
```

```python
import jax
import numpy as np
import jax.numpy as jnp
from jax import lax
from jax.sharding import PartitionSpec as P


def with_halo(cells, axis, dim, width=1):
    count = lax.axis_size(axis)
    ends = count - 1
    head = lax.slice_in_dim(cells, 0, width, axis=dim)
    tail = lax.slice_in_dim(cells, cells.shape[dim] - width, cells.shape[dim], axis=dim)
    return jnp.concatenate(
        [
            lax.ppermute(tail, axis, [(i, (i + 1) % count) for i in range(ends)]),
            cells,
            lax.ppermute(head, axis, [((i + 1) % count, i) for i in range(ends)]),
        ],
        axis=dim,
    )


def lane_shift(field, dm):
    if dm == 0:
        return field
    zeros = jnp.zeros(field.shape[:-1] + (1,), field.dtype)
    if dm < 0:
        return jnp.concatenate([zeros, field[..., :-1]], axis=-1)
    return jnp.concatenate([field[..., 1:], zeros], axis=-1)


def phase_patches(field):
    phases, depth, height, _, width = field.shape
    depth -= 2
    field = jnp.pad(field, ((0, 0), (0, 0), (1, 1), (0, 0), (0, 0)))
    sources = {}
    out = []
    for r in range(phases):
        taps = []
        for a in range(3):
            for b in range(3):
                for e in range(3):
                    key = ((r + e - 1) % phases, (r + e - 1) // phases)
                    if key not in sources:
                        sources[key] = lane_shift(field[key[0]], key[1])
                    taps.append(sources[key][a : a + depth, b : b + height])
        out.append(jnp.concatenate(taps, axis=2))
    return jnp.stack(out, axis=0)


def conv_taps(kern, patches):
    return jnp.einsum("ok,rxykm->orxym", kern.reshape(kern.shape[0], -1), patches, preferred_element_type=jnp.float32)


def grad_taps(grads, patches):
    return jnp.einsum("orxym,rxykm->ok", grads, patches, preferred_element_type=jnp.float32)


def pool(field):
    chan, phases, depth, height, width = field.shape
    blocks = field.reshape(chan, phases // 2, 2, depth // 2, 2, height // 2, 2, width)
    return blocks.sum(axis=(2, 4, 6)) * 0.125


def upsample(field, phases):
    return jnp.repeat(jnp.repeat(jnp.repeat(field, 2, axis=1), 2, axis=2), 2, axis=3)


def silu_slope(value):
    sig = jax.nn.sigmoid(value)
    return sig * (1.0 + value * (1.0 - sig))


def butterfly_sum(rows, axes):
    for axis in axes:
        count = lax.axis_size(axis)
        step = 1
        while step < count:
            rows = rows + lax.ppermute(rows, axis, [(i, i ^ step) for i in range(count)])
            step *= 2
    return rows


def tap_major(kern):
    return jnp.transpose(kern, (0, 2, 3, 4, 1)).reshape(kern.shape[0], 27, kern.shape[1])


def tap_minor(grad, chan):
    return jnp.transpose(grad.reshape(grad.shape[0], 3, 3, 3, chan), (0, 4, 1, 2, 3))


def phase_select(phases):
    sel = np.zeros((phases, 3, phases, 3), np.float32)
    for r in range(phases):
        for e in range(3):
            sel[r, (r + e - 1) // phases + 1, (r + e - 1) % phases, e] = 1.0
    return sel


def merged_patches(field):
    depth, height = field.shape[0] - 2, field.shape[1]
    field = jnp.pad(field, ((0, 0), (1, 1), (0, 0), (0, 0)))
    shifted = [lane_shift(field, dm) for dm in (-1, 0, 1)]
    taps = []
    for a in range(3):
        for b in range(3):
            for dm in range(3):
                taps.append(shifted[dm][a : a + depth, b : b + height])
    return jnp.concatenate(taps, axis=2)


def merged_kernel(kern, phases):
    sel = phase_select(phases)
    taps = jnp.transpose(kern.astype(jnp.float32), (0, 2, 3, 1, 4))
    full = taps[:, None, :, :, None, None, :, :] * sel[None, :, None, None, :, :, None, :]
    return full.sum(axis=-1).reshape(kern.shape[0], phases, -1).astype(kern.dtype)


def merged_grad(grads, chan, phases):
    sel = phase_select(phases)
    full = grads.reshape(grads.shape[0], phases, 3, 3, 3, phases, chan)
    summed = (full[..., None] * sel[None, :, None, None, :, :, None, :]).sum(axis=(1, 4, 5))
    return jnp.transpose(summed, (0, 1, 2, 4, 3)).reshape(grads.shape[0], -1)


def shards(volume, cotangent, w_first, b_first, w_second, b_second):
    sample = volume[0]
    cot = cotangent[0]
    chan0, _, height, width = sample.shape
    depth = sample.shape[1]
    halo = with_halo(sample, "space", 1, 3)
    merged = jnp.transpose(halo.reshape(chan0, halo.shape[1], height, width // 4, 4), (1, 2, 4, 0, 3))
    patches_wide = merged_patches(merged.reshape(halo.shape[1], height, 4 * chan0, width // 4))
    pre_wide = (
        jnp.einsum(
            "ork,xykm->orxym", merged_kernel(w_first, 4), patches_wide, preferred_element_type=jnp.float32
        )
        + b_first[:, None, None, None, None]
    )
    pooled_wide = pool(jax.nn.silu(pre_wide)).astype(jnp.bfloat16)
    place = lax.axis_index("space")
    rows = jnp.arange(pooled_wide.shape[2])
    inside = ((rows > 0) | (place > 0)) & ((rows < pooled_wide.shape[2] - 1) | (place < lax.axis_size("space") - 1))
    pooled_wide = jnp.where(inside[None, None, :, None, None], pooled_wide, jnp.zeros_like(pooled_wide))
    pooled_halo = jnp.transpose(pooled_wide, (1, 2, 3, 0, 4))
    pre_first = pre_wide[:, :, 2 : 2 + depth]
    patches_first = patches_wide[2 : 2 + depth]
    patches_second = phase_patches(pooled_halo)
    pre_second = conv_taps(tap_major(w_second), patches_second) + b_second[:, None, None, None, None]
    output = pool(jax.nn.silu(pre_second))[:, 0].astype(jnp.bfloat16)
    grad_second = (
        upsample(cot.astype(jnp.float32)[:, None], 2) * 0.125 * silu_slope(pre_second)
    ).astype(jnp.bfloat16)
    grad_w2 = grad_taps(grad_second, patches_second)
    grad_b2 = jnp.sum(grad_second.astype(jnp.float32), axis=(1, 2, 3, 4))
    grad_halo = jnp.transpose(with_halo(grad_second, "space", 2), (1, 2, 3, 0, 4))
    flipped = tap_major(jnp.transpose(jnp.flip(w_second, (2, 3, 4)), (1, 0, 2, 3, 4)))
    back = conv_taps(flipped, phase_patches(grad_halo))
    grad_first = (upsample(back, 4) * 0.125 * silu_slope(pre_first)).astype(jnp.bfloat16)
    grad_w1 = merged_grad(
        lax.optimization_barrier(
            jnp.einsum(
                "qxym,xykm->qk",
                grad_first.reshape((-1,) + grad_first.shape[2:]),
                patches_first,
                preferred_element_type=jnp.float32,
            )
        ).reshape(grad_first.shape[0], grad_first.shape[1], -1),
        chan0,
        4,
    )
    grad_b1 = jnp.sum(grad_first.astype(jnp.float32), axis=(1, 2, 3, 4))
    chan1 = w_second.shape[1]
    rows_w2, lanes_w2 = grad_w2.shape
    side = grad_w1.reshape(rows_w2, -1)
    lanes_w1 = side.shape[1]
    packed = jnp.concatenate(
        [
            grad_w2,
            side,
            grad_b2[:, None],
            jnp.pad(grad_b1, (0, rows_w2 - grad_b1.shape[0]))[:, None],
        ],
        axis=1,
    )
    totals = butterfly_sum(packed, ("space", "dp"))
    out_w2 = tap_minor(totals[:, :lanes_w2], chan1)
    out_w1 = tap_minor(totals[:, lanes_w2 : lanes_w2 + lanes_w1].reshape(grad_w1.shape), chan0)
    out_b2 = totals[:, lanes_w2 + lanes_w1]
    out_b1 = totals[: grad_b1.shape[0], lanes_w2 + lanes_w1 + 1]
    return (output[None], out_w1, out_b1, out_w2, out_b2)


def solution(mesh):
    placed = (
        P("dp", None, "space", None, None),
        P("dp", None, "space", None, None),
        P(),
        P(),
        P(),
        P(),
    )
    return jax.shard_map(
        shards,
        mesh=mesh,
        in_specs=placed,
        out_specs=(P("dp", None, "space", None, None), P(), P(), P(), P()),
        check_vma=False,
    )
```

```python
import jax
import numpy as np
import jax.numpy as jnp
from jax import lax
from jax.sharding import PartitionSpec as P


def with_halo(cells, axis, dim, width=1):
    count = lax.axis_size(axis)
    ends = count - 1
    head = lax.slice_in_dim(cells, 0, width, axis=dim)
    tail = lax.slice_in_dim(cells, cells.shape[dim] - width, cells.shape[dim], axis=dim)
    return jnp.concatenate(
        [
            lax.ppermute(tail, axis, [(i, (i + 1) % count) for i in range(ends)]),
            cells,
            lax.ppermute(head, axis, [((i + 1) % count, i) for i in range(ends)]),
        ],
        axis=dim,
    )


def lane_shift(field, dm):
    if dm == 0:
        return field
    zeros = jnp.zeros(field.shape[:-1] + (1,), field.dtype)
    if dm < 0:
        return jnp.concatenate([zeros, field[..., :-1]], axis=-1)
    return jnp.concatenate([field[..., 1:], zeros], axis=-1)


def phase_patches(field):
    phases, depth, height, _, width = field.shape
    depth -= 2
    field = jnp.pad(field, ((0, 0), (0, 0), (1, 1), (0, 0), (0, 0)))
    sources = {}
    out = []
    for r in range(phases):
        taps = []
        for a in range(3):
            for b in range(3):
                for e in range(3):
                    key = ((r + e - 1) % phases, (r + e - 1) // phases)
                    if key not in sources:
                        sources[key] = lane_shift(field[key[0]], key[1])
                    taps.append(sources[key][a : a + depth, b : b + height])
        out.append(jnp.concatenate(taps, axis=2))
    return jnp.stack(out, axis=0)


def conv_taps(kern, patches):
    return jnp.einsum("ok,rxykm->orxym", kern.reshape(kern.shape[0], -1), patches, preferred_element_type=jnp.float32)


def grad_taps(grads, patches):
    return jnp.einsum("orxym,rxykm->ok", grads, patches, preferred_element_type=jnp.float32)


def pool(field):
    chan, phases, depth, height, width = field.shape
    blocks = field.reshape(chan, phases // 2, 2, depth // 2, 2, height // 2, 2, width)
    return blocks.sum(axis=(2, 4, 6)) * 0.125


def upsample(field, phases):
    return jnp.repeat(jnp.repeat(jnp.repeat(field, 2, axis=1), 2, axis=2), 2, axis=3)


def sigmoid(value):
    return 0.5 + 0.5 * jnp.tanh(0.5 * value)


def silu(value):
    return value * sigmoid(value)


def silu_slope(value):
    sig = sigmoid(value)
    return sig * (1.0 + value * (1.0 - sig))


def butterfly_sum(rows, axes):
    for axis in axes:
        count = lax.axis_size(axis)
        step = 1
        while step < count:
            rows = rows + lax.ppermute(rows, axis, [(i, i ^ step) for i in range(count)])
            step *= 2
    return rows


def tap_major(kern):
    return jnp.transpose(kern, (0, 2, 3, 4, 1)).reshape(kern.shape[0], 27, kern.shape[1])


def tap_minor(grad, chan):
    return jnp.transpose(grad.reshape(grad.shape[0], 3, 3, 3, chan), (0, 4, 1, 2, 3))


def phase_select(phases):
    sel = np.zeros((phases, 3, phases, 3), np.float32)
    for r in range(phases):
        for e in range(3):
            sel[r, (r + e - 1) // phases + 1, (r + e - 1) % phases, e] = 1.0
    return sel


def merged_patches(field):
    depth, height = field.shape[0] - 2, field.shape[1]
    field = jnp.pad(field, ((0, 0), (1, 1), (0, 0), (0, 0)))
    shifted = [lane_shift(field, dm) for dm in (-1, 0, 1)]
    taps = []
    for a in range(3):
        for b in range(3):
            for dm in range(3):
                taps.append(shifted[dm][a : a + depth, b : b + height])
    return jnp.concatenate(taps, axis=2)


def merged_kernel(kern, phases):
    sel = phase_select(phases)
    taps = jnp.transpose(kern.astype(jnp.float32), (0, 2, 3, 1, 4))
    full = taps[:, None, :, :, None, None, :, :] * sel[None, :, None, None, :, :, None, :]
    return full.sum(axis=-1).reshape(kern.shape[0], phases, -1).astype(kern.dtype)


def merged_grad(grads, chan, phases):
    sel = phase_select(phases)
    full = grads.reshape(grads.shape[0], phases, 3, 3, 3, phases, chan)
    summed = (full[..., None] * sel[None, :, None, None, :, :, None, :]).sum(axis=(1, 4, 5))
    return jnp.transpose(summed, (0, 1, 2, 4, 3)).reshape(grads.shape[0], -1)


def shards(volume, cotangent, w_first, b_first, w_second, b_second):
    sample = volume[0]
    cot = cotangent[0]
    chan0, _, height, width = sample.shape
    depth = sample.shape[1]
    halo = with_halo(sample, "space", 1, 3)
    merged = jnp.transpose(halo.reshape(chan0, halo.shape[1], height, width // 4, 4), (1, 2, 4, 0, 3))
    patches_wide = merged_patches(merged.reshape(halo.shape[1], height, 4 * chan0, width // 4))
    pre_wide = (
        jnp.einsum(
            "ork,xykm->orxym", merged_kernel(w_first, 4), patches_wide, preferred_element_type=jnp.float32
        )
        + b_first[:, None, None, None, None]
    )
    pooled_wide = pool(silu(pre_wide)).astype(jnp.bfloat16)
    place = lax.axis_index("space")
    rows = jnp.arange(pooled_wide.shape[2])
    inside = ((rows > 0) | (place > 0)) & ((rows < pooled_wide.shape[2] - 1) | (place < lax.axis_size("space") - 1))
    pooled_wide = jnp.where(inside[None, None, :, None, None], pooled_wide, jnp.zeros_like(pooled_wide))
    pooled_halo = jnp.transpose(pooled_wide, (1, 2, 3, 0, 4))
    pre_first = pre_wide[:, :, 2 : 2 + depth]
    patches_first = patches_wide[2 : 2 + depth]
    patches_second = phase_patches(pooled_halo)
    pre_second = conv_taps(tap_major(w_second), patches_second) + b_second[:, None, None, None, None]
    output = pool(silu(pre_second))[:, 0].astype(jnp.bfloat16)
    grad_second = (
        upsample(cot.astype(jnp.float32)[:, None], 2) * 0.125 * silu_slope(pre_second)
    ).astype(jnp.bfloat16)
    grad_w2 = grad_taps(grad_second, patches_second)
    grad_b2 = jnp.sum(grad_second.astype(jnp.float32), axis=(1, 2, 3, 4))
    grad_halo = jnp.transpose(with_halo(grad_second, "space", 2), (1, 2, 3, 0, 4))
    flipped = tap_major(jnp.transpose(jnp.flip(w_second, (2, 3, 4)), (1, 0, 2, 3, 4)))
    back = conv_taps(flipped, phase_patches(grad_halo))
    grad_first = (upsample(back, 4) * 0.125 * silu_slope(pre_first)).astype(jnp.bfloat16)
    grad_w1 = merged_grad(
        jnp.einsum("orxym,xykm->ork", grad_first, patches_first, preferred_element_type=jnp.float32),
        chan0,
        4,
    )
    grad_b1 = jnp.sum(grad_first.astype(jnp.float32), axis=(1, 2, 3, 4))
    chan1 = w_second.shape[1]
    rows_w2, lanes_w2 = grad_w2.shape
    side = grad_w1.reshape(rows_w2, -1)
    lanes_w1 = side.shape[1]
    packed = jnp.concatenate(
        [
            grad_w2,
            side,
            grad_b2[:, None],
            jnp.pad(grad_b1, (0, rows_w2 - grad_b1.shape[0]))[:, None],
        ],
        axis=1,
    )
    totals = butterfly_sum(packed, ("space", "dp"))
    out_w2 = tap_minor(totals[:, :lanes_w2], chan1)
    out_w1 = tap_minor(totals[:, lanes_w2 : lanes_w2 + lanes_w1].reshape(grad_w1.shape), chan0)
    out_b2 = totals[:, lanes_w2 + lanes_w1]
    out_b1 = totals[: grad_b1.shape[0], lanes_w2 + lanes_w1 + 1]
    return (output[None], out_w1, out_b1, out_w2, out_b2)


def solution(mesh):
    placed = (
        P("dp", None, "space", None, None),
        P("dp", None, "space", None, None),
        P(),
        P(),
        P(),
        P(),
    )
    return jax.shard_map(
        shards,
        mesh=mesh,
        in_specs=placed,
        out_specs=(P("dp", None, "space", None, None), P(), P(), P(), P()),
        check_vma=False,
    )
```

```python
import jax
import numpy as np
import jax.numpy as jnp
from jax import lax
from jax.sharding import PartitionSpec as P


def with_halo(cells, axis, dim, width=1):
    count = lax.axis_size(axis)
    ends = count - 1
    head = lax.slice_in_dim(cells, 0, width, axis=dim)
    tail = lax.slice_in_dim(cells, cells.shape[dim] - width, cells.shape[dim], axis=dim)
    return jnp.concatenate(
        [
            lax.ppermute(tail, axis, [(i, (i + 1) % count) for i in range(ends)]),
            cells,
            lax.ppermute(head, axis, [((i + 1) % count, i) for i in range(ends)]),
        ],
        axis=dim,
    )


def lane_shift(field, dm):
    if dm == 0:
        return field
    zeros = jnp.zeros(field.shape[:-1] + (1,), field.dtype)
    if dm < 0:
        return jnp.concatenate([zeros, field[..., :-1]], axis=-1)
    return jnp.concatenate([field[..., 1:], zeros], axis=-1)


def phase_patches(field):
    phases, depth, height, _, width = field.shape
    depth -= 2
    field = jnp.pad(field, ((0, 0), (0, 0), (1, 1), (0, 0), (0, 0)))
    sources = {}
    out = []
    for r in range(phases):
        taps = []
        for a in range(3):
            for b in range(3):
                for e in range(3):
                    key = ((r + e - 1) % phases, (r + e - 1) // phases)
                    if key not in sources:
                        sources[key] = lane_shift(field[key[0]], key[1])
                    taps.append(sources[key][a : a + depth, b : b + height])
        out.append(jnp.concatenate(taps, axis=2))
    return jnp.stack(out, axis=0)


def conv_taps(kern, patches):
    return jnp.einsum("ok,rxykm->orxym", kern.reshape(kern.shape[0], -1), patches, preferred_element_type=jnp.float32)


def grad_taps(grads, patches):
    return jnp.einsum("orxym,rxykm->ok", grads, patches, preferred_element_type=jnp.float32)


def pool(field):
    chan, phases, depth, height, width = field.shape
    blocks = field.reshape(chan, phases // 2, 2, depth // 2, 2, height // 2, 2, width)
    return blocks.sum(axis=(2, 4, 6)) * 0.125


def upsample(field, phases):
    return jnp.repeat(jnp.repeat(jnp.repeat(field, 2, axis=1), 2, axis=2), 2, axis=3)


def silu_slope(value):
    sig = jax.nn.sigmoid(value)
    return sig * (1.0 + value * (1.0 - sig))


def butterfly_sum(rows, axes):
    for axis in axes:
        count = lax.axis_size(axis)
        step = 1
        while step < count:
            rows = rows + lax.ppermute(rows, axis, [(i, i ^ step) for i in range(count)])
            step *= 2
    return rows


def tap_major(kern):
    return jnp.transpose(kern, (0, 2, 3, 4, 1)).reshape(kern.shape[0], 27, kern.shape[1])


def tap_minor(grad, chan):
    return jnp.transpose(grad.reshape(grad.shape[0], 3, 3, 3, chan), (0, 4, 1, 2, 3))


def phase_select(phases):
    sel = np.zeros((phases, 3, phases, 3), np.float32)
    for r in range(phases):
        for e in range(3):
            sel[r, (r + e - 1) // phases + 1, (r + e - 1) % phases, e] = 1.0
    return sel


def merged_patches(field):
    depth, height = field.shape[0] - 2, field.shape[1]
    field = jnp.pad(field, ((0, 0), (1, 1), (0, 0), (0, 0)))
    shifted = [lane_shift(field, dm) for dm in (-1, 0, 1)]
    taps = []
    for a in range(3):
        for b in range(3):
            for dm in range(3):
                taps.append(shifted[dm][a : a + depth, b : b + height])
    return jnp.concatenate(taps, axis=2)


def merged_kernel(kern, phases):
    sel = phase_select(phases)
    taps = jnp.transpose(kern.astype(jnp.float32), (0, 2, 3, 1, 4))
    full = taps[:, None, :, :, None, None, :, :] * sel[None, :, None, None, :, :, None, :]
    return full.sum(axis=-1).reshape(kern.shape[0], phases, -1).astype(kern.dtype)


def merged_grad(grads, chan, phases):
    sel = phase_select(phases)
    full = grads.reshape(grads.shape[0], phases, 3, 3, 3, phases, chan)
    summed = (full[..., None] * sel[None, :, None, None, :, :, None, :]).sum(axis=(1, 4, 5))
    return jnp.transpose(summed, (0, 1, 2, 4, 3)).reshape(grads.shape[0], -1)


def shards(volume, cotangent, w_first, b_first, w_second, b_second):
    sample = volume[0]
    cot = cotangent[0]
    chan0, _, height, width = sample.shape
    depth = sample.shape[1]
    halo = with_halo(sample, "space", 1, 3)
    merged = jnp.transpose(halo.reshape(chan0, halo.shape[1], height, width // 4, 4), (1, 2, 4, 0, 3))
    patches_wide = merged_patches(merged.reshape(halo.shape[1], height, 4 * chan0, width // 4))
    pre_wide = (
        jnp.einsum(
            "ork,xykm->orxym", merged_kernel(w_first, 4), patches_wide, preferred_element_type=jnp.float32
        )
        + b_first[:, None, None, None, None]
    )
    pooled_wide = pool(jax.nn.silu(pre_wide)).astype(jnp.bfloat16)
    place = lax.axis_index("space")
    rows = jnp.arange(pooled_wide.shape[2])
    inside = ((rows > 0) | (place > 0)) & ((rows < pooled_wide.shape[2] - 1) | (place < lax.axis_size("space") - 1))
    pooled_wide = jnp.where(inside[None, None, :, None, None], pooled_wide, jnp.zeros_like(pooled_wide))
    pooled_halo = jnp.transpose(pooled_wide, (1, 2, 3, 0, 4))
    pre_first = pre_wide[:, :, 2 : 2 + depth]
    patches_first = patches_wide[2 : 2 + depth]
    patches_second = phase_patches(pooled_halo)
    pre_second = conv_taps(tap_major(w_second), patches_second) + b_second[:, None, None, None, None]
    output = pool(jax.nn.silu(pre_second))[:, 0].astype(jnp.bfloat16)
    grad_second = (
        upsample(cot.astype(jnp.float32)[:, None], 2) * 0.125 * silu_slope(pre_second)
    ).astype(jnp.bfloat16)
    grad_w2 = grad_taps(grad_second, patches_second)
    grad_b2 = jnp.sum(grad_second.astype(jnp.float32), axis=(1, 2, 3, 4))
    grad_halo = jnp.transpose(with_halo(grad_second, "space", 2), (1, 2, 3, 0, 4))
    flipped = tap_major(jnp.transpose(jnp.flip(w_second, (2, 3, 4)), (1, 0, 2, 3, 4)))
    back = conv_taps(flipped, phase_patches(grad_halo))
    grad_first = (upsample(back, 4) * 0.125 * silu_slope(pre_first)).astype(jnp.bfloat16)
    grad_w1 = merged_grad(
        jnp.einsum("orxym,xykm->ork", grad_first, patches_first, preferred_element_type=jnp.float32),
        chan0,
        4,
    )
    grad_b1 = jnp.sum(grad_first.astype(jnp.float32), axis=(1, 2, 3, 4))
    chan1 = w_second.shape[1]
    rows_w2, lanes_w2 = grad_w2.shape
    side = grad_w1.reshape(rows_w2, -1)
    lanes_w1 = side.shape[1]
    packed = jnp.concatenate(
        [
            grad_w2,
            side,
            grad_b2[:, None],
            jnp.pad(grad_b1, (0, rows_w2 - grad_b1.shape[0]))[:, None],
        ],
        axis=1,
    )
    totals = butterfly_sum(packed, ("dp", "space"))
    out_w2 = tap_minor(totals[:, :lanes_w2], chan1)
    out_w1 = tap_minor(totals[:, lanes_w2 : lanes_w2 + lanes_w1].reshape(grad_w1.shape), chan0)
    out_b2 = totals[:, lanes_w2 + lanes_w1]
    out_b1 = totals[: grad_b1.shape[0], lanes_w2 + lanes_w1 + 1]
    return (output[None], out_w1, out_b1, out_w2, out_b2)


def solution(mesh):
    placed = (
        P("dp", None, "space", None, None),
        P("dp", None, "space", None, None),
        P(),
        P(),
        P(),
        P(),
    )
    return jax.shard_map(
        shards,
        mesh=mesh,
        in_specs=placed,
        out_specs=(P("dp", None, "space", None, None), P(), P(), P(), P()),
        check_vma=False,
    )
```

```python
import jax
import numpy as np
import jax.numpy as jnp
from jax import lax
from jax.sharding import PartitionSpec as P


def with_halo(cells, axis, dim, width=1):
    count = lax.axis_size(axis)
    ends = count - 1
    head = lax.slice_in_dim(cells, 0, width, axis=dim)
    tail = lax.slice_in_dim(cells, cells.shape[dim] - width, cells.shape[dim], axis=dim)
    return jnp.concatenate(
        [
            lax.ppermute(tail, axis, [(i, (i + 1) % count) for i in range(ends)]),
            cells,
            lax.ppermute(head, axis, [((i + 1) % count, i) for i in range(ends)]),
        ],
        axis=dim,
    )


def lane_shift(field, dm):
    if dm == 0:
        return field
    zeros = jnp.zeros(field.shape[:-1] + (1,), field.dtype)
    if dm < 0:
        return jnp.concatenate([zeros, field[..., :-1]], axis=-1)
    return jnp.concatenate([field[..., 1:], zeros], axis=-1)


def phase_patches(field):
    phases, depth, height, _, width = field.shape
    depth -= 2
    field = jnp.pad(field, ((0, 0), (0, 0), (1, 1), (0, 0), (0, 0)))
    sources = {}
    out = []
    for r in range(phases):
        taps = []
        for a in range(3):
            for b in range(3):
                for e in range(3):
                    key = ((r + e - 1) % phases, (r + e - 1) // phases)
                    if key not in sources:
                        sources[key] = lane_shift(field[key[0]], key[1])
                    taps.append(sources[key][a : a + depth, b : b + height])
        out.append(jnp.concatenate(taps, axis=2))
    return jnp.stack(out, axis=0)


def conv_taps(kern, patches):
    return jnp.einsum("ok,rxykm->orxym", kern.reshape(kern.shape[0], -1), patches, preferred_element_type=jnp.float32)


def grad_taps(grads, patches):
    return jnp.einsum("orxym,rxykm->ok", grads, patches, preferred_element_type=jnp.float32)


def pool(field):
    chan, phases, depth, height, width = field.shape
    blocks = field.reshape(chan, phases // 2, 2, depth // 2, 2, height // 2, 2, width)
    return blocks.sum(axis=(2, 4, 6)) * 0.125


def upsample(field, phases):
    return jnp.repeat(jnp.repeat(jnp.repeat(field, 2, axis=1), 2, axis=2), 2, axis=3)


def silu_slope(value):
    sig = jax.nn.sigmoid(value)
    return sig * (1.0 + value * (1.0 - sig))


def butterfly_sum(rows, axes):
    for axis in axes:
        count = lax.axis_size(axis)
        step = 1
        while step < count:
            rows = rows + lax.ppermute(rows, axis, [(i, i ^ step) for i in range(count)])
            step *= 2
    return rows


def tap_major(kern):
    return jnp.transpose(kern, (0, 2, 3, 4, 1)).reshape(kern.shape[0], 27, kern.shape[1])


def tap_minor(grad, chan):
    return jnp.transpose(grad.reshape(grad.shape[0], 3, 3, 3, chan), (0, 4, 1, 2, 3))


def phase_select(phases):
    sel = np.zeros((phases, 3, phases, 3), np.float32)
    for r in range(phases):
        for e in range(3):
            sel[r, (r + e - 1) // phases + 1, (r + e - 1) % phases, e] = 1.0
    return sel


def merged_patches(field):
    depth, height = field.shape[0] - 2, field.shape[1]
    field = jnp.pad(field, ((0, 0), (1, 1), (0, 0), (0, 0)))
    shifted = [lane_shift(field, dm) for dm in (-1, 0, 1)]
    taps = []
    for a in range(3):
        for b in range(3):
            for dm in range(3):
                taps.append(shifted[dm][a : a + depth, b : b + height])
    return jnp.concatenate(taps, axis=2)


def merged_kernel(kern, phases):
    sel = phase_select(phases)
    taps = jnp.transpose(kern.astype(jnp.float32), (0, 2, 3, 1, 4))
    full = taps[:, None, :, :, None, None, :, :] * sel[None, :, None, None, :, :, None, :]
    return full.sum(axis=-1).reshape(kern.shape[0], phases, -1).astype(kern.dtype)


def merged_grad(grads, chan, phases):
    sel = phase_select(phases)
    full = grads.reshape(grads.shape[0], phases, 3, 3, 3, phases, chan)
    summed = (full[..., None] * sel[None, :, None, None, :, :, None, :]).sum(axis=(1, 4, 5))
    return jnp.transpose(summed, (0, 1, 2, 4, 3)).reshape(grads.shape[0], -1)


def shards(volume, cotangent, w_first, b_first, w_second, b_second):
    sample = volume[0]
    cot = cotangent[0]
    chan0, _, height, width = sample.shape
    depth = sample.shape[1]
    halo = with_halo(sample, "space", 1, 3)
    merged = jnp.transpose(halo.reshape(chan0, halo.shape[1], height, width // 4, 4), (1, 2, 4, 0, 3))
    patches_wide = merged_patches(merged.reshape(halo.shape[1], height, 4 * chan0, width // 4))
    pre_wide = (
        jnp.einsum(
            "ork,xykm->orxym", merged_kernel(w_first, 4), patches_wide, preferred_element_type=jnp.float32
        )
        + b_first[:, None, None, None, None]
    )
    pooled_wide = pool(jax.nn.silu(pre_wide)).astype(jnp.bfloat16)
    place = lax.axis_index("space")
    rows = jnp.arange(pooled_wide.shape[2])
    inside = ((rows > 0) | (place > 0)) & ((rows < pooled_wide.shape[2] - 1) | (place < lax.axis_size("space") - 1))
    pooled_wide = jnp.where(inside[None, None, :, None, None], pooled_wide, jnp.zeros_like(pooled_wide))
    pooled_halo = jnp.transpose(pooled_wide, (1, 2, 3, 0, 4))
    pre_first = pre_wide[:, :, 2 : 2 + depth]
    patches_first = patches_wide[2 : 2 + depth]
    patches_second = phase_patches(pooled_halo)
    pre_second = conv_taps(tap_major(w_second), patches_second) + b_second[:, None, None, None, None]
    output = pool(jax.nn.silu(pre_second))[:, 0].astype(jnp.bfloat16)
    grad_second = (
        upsample(cot.astype(jnp.float32)[:, None], 2) * 0.125 * silu_slope(pre_second)
    ).astype(jnp.bfloat16)
    grad_w2 = grad_taps(grad_second, patches_second)
    grad_b2 = jnp.sum(grad_second.astype(jnp.float32), axis=(1, 2, 3, 4))
    grad_halo = jnp.transpose(with_halo(grad_second, "space", 2), (1, 2, 3, 0, 4))
    flipped = tap_major(jnp.transpose(jnp.flip(w_second, (2, 3, 4)), (1, 0, 2, 3, 4)))
    back = conv_taps(flipped, phase_patches(grad_halo))
    grad_first = (upsample(back, 4) * 0.125 * silu_slope(pre_first)).astype(jnp.bfloat16)
    grad_w1 = merged_grad(
        jnp.einsum("orxym,xykm->ork", grad_first, patches_first, preferred_element_type=jnp.float32),
        chan0,
        4,
    )
    grad_b1 = jnp.sum(grad_first.astype(jnp.float32), axis=(1, 2, 3, 4))
    chan1 = w_second.shape[1]
    rows_w2, lanes_w2 = grad_w2.shape
    side = grad_w1.reshape(rows_w2, -1)
    lanes_w1 = side.shape[1]
    packed = jnp.concatenate(
        [
            grad_w2,
            side,
            grad_b2[:, None],
            jnp.pad(grad_b1, (0, rows_w2 - grad_b1.shape[0]))[:, None],
        ],
        axis=1,
    )
    totals = butterfly_sum(packed, ("dp", "space"))
    out_w2 = tap_minor(totals[:, :lanes_w2], chan1)
    out_w1 = tap_minor(totals[:, lanes_w2 : lanes_w2 + lanes_w1].reshape(grad_w1.shape), chan0)
    bias_rows = totals[:, lanes_w2 + lanes_w1 : lanes_w2 + lanes_w1 + 2].T
    out_b2 = bias_rows[0]
    out_b1 = bias_rows[1, : grad_b1.shape[0]]
    return (output[None], out_w1, out_b1, out_w2, out_b2)


def solution(mesh):
    placed = (
        P("dp", None, "space", None, None),
        P("dp", None, "space", None, None),
        P(),
        P(),
        P(),
        P(),
    )
    return jax.shard_map(
        shards,
        mesh=mesh,
        in_specs=placed,
        out_specs=(P("dp", None, "space", None, None), P(), P(), P(), P()),
        check_vma=False,
    )
```
